256 devices in a mesh: gz: 16 (over y, x), xy: 16 (over z, core).
Axes of the slice: x: 4, y: 4, z: 8, core: 2. Of those that a mesh axis runs over, the one named last changes fastest.
Arguments:
- residual_in: float32 [144, 128, 16, 128], P(None, 'gz', 'xy'), may hold values from -75 to 75
- ritz_vector: float32 [144, 128, 16, 128], P(None, 'gz', 'xy'), may hold values from -14.4 to 14.4
- density: float32 [128, 16, 128], P('gz', 'xy'), may hold values from 0 to 1
- pml_flags: int32 [128, 16, 128], P('gz', 'xy'), may hold values 0 or 1
- design_mask: int32 [128, 16, 128], P('gz', 'xy'), may hold values 0 or 1
- k_base: float32 [144, 144], replicated, may hold values from -0.5 to 4.5
- k_rho: float32 [144, 144], replicated, may hold values from -0.5 to 0.5
- k_pml: float32 [144, 144], replicated, may hold values from -0.5 to 0.5
- k_face: float32 [6, 144, 144], replicated, may hold values from -0.5 to 0.5
- shift_re: float32 [], replicated, may hold values from 0.5 to 2
- shift_im: float32 [], replicated, may hold values from 0.2 to 1
Outputs:
- correction: float32 [144, 128, 16, 128], P(None, 'gz', 'xy')
- filtered: float32 [128, 16, 128], P('gz', 'xy')
The draws below stay inside these ranges and needn't reach their ends.
All inputs are finite; a program needn't handle non-finite values. No bound on the sum of `pml_flags` or of `design_mask` on one device may be relied on, other than what follows from the above.
Results may differ from the reference program's by a relative error of at most 0.0055.
Values sent between devices are 32-bit elements; how exact they have to be, the bound alone decides.
No kernel may reach another device: no remote copies, remote signals or barrier semaphores. Data moves between devices by JAX's collectives and lax.ppermute only.
A program may use at most 64 MiB of HBM per device.

```python
import math
import jax
import jax.numpy as jnp
from jax import lax

B = 144
TX = 4
EY = 8
EX = 16
TY = 4
TILES = 16
NZ = 128
ELEMS = 262144


mean_diagonal = 3.0 / math.log(4.0)


def ritz_common(key):
    values = jax.random.normal(jax.random.fold_in(key, 101), (B, 1, 1, 1), jnp.float32)
    return 0.8 * jnp.clip(values, -3.0, 3.0)


def depth_profile():
    layers = jnp.arange(NZ, dtype=jnp.float32)
    return (1.0 + layers / (NZ - 1.0))[None, :, None, None]


def random_field(key, number):
    field_shape = (B, NZ, TILES, EY * EX)
    return jnp.clip(jax.random.normal(jax.random.fold_in(key, number), field_shape, jnp.float32), -4.0, 4.0)


def ritz_field(key):
    return (ritz_common(key) + random_field(key, 102)) * depth_profile()


def base_diagonal(key):
    return jnp.exp(jax.random.uniform(jax.random.fold_in(key, 201), (B,), jnp.float32, 0.0, math.log(4.0)))


def draw_k_base(key, part):
    diagonal_part = base_diagonal(key)
    coupling = jnp.clip(jax.random.normal(jax.random.fold_in(key, 202), (B, B), jnp.float32) / 12.0, -0.5, 0.5)
    return coupling + jnp.eye(B, dtype=jnp.float32) * diagonal_part[None, :]


def draw_ritz_vector(key, part):
    return ritz_field(key)


def draw_residual_in(key, part):
    ritz = ritz_field(key)
    half_rows = B // 2
    turned = jnp.concatenate([-ritz[half_rows:], ritz[:half_rows]], axis=0)
    amplitude = jax.random.uniform(jax.random.fold_in(key, 301), (), jnp.float32, 0.5, 1.5)
    rotation = jax.random.uniform(jax.random.fold_in(key, 302), (), jnp.float32, -math.pi, math.pi)
    tilted = 1.5 * ritz_common(key) * (base_diagonal(key) - mean_diagonal)[:, None, None, None]
    aligned = amplitude * (jnp.cos(rotation) * ritz + jnp.sin(rotation) * turned)
    return (random_field(key, 303) + tilted) * depth_profile() + aligned


def with_ends(entries, rng, low, high):
    longest = entries.shape.index(max(entries.shape))
    spots = []
    for shift in (0, 1):
        where = [jax.random.randint(jax.random.fold_in(rng, axis), (), 0, length) for axis, length in enumerate(entries.shape)]
        where[longest] = (where[longest] + shift) % entries.shape[longest]
        spots.append(tuple(where))
    return entries.at[spots[0]].set(low).at[spots[1]].set(high)


def steps_of(rng, extent, cuts, smallest, largest):
    def one(position, shards_of):
        heights = jax.random.uniform(jax.random.fold_in(jax.random.fold_in(rng, 6), position), (shards_of,), jnp.float32, smallest / len(cuts), largest / len(cuts))
        return jnp.repeat(jnp.exp(heights), extent[position] // shards_of).reshape((-1,) + (1,) * (len(extent) - position - 1))

    level = one(*cuts[0])
    for cut in cuts[1:]:
        level = level * one(*cut)
    return level


def noise(key, extent, spread, bound, kind=jnp.bfloat16):
    array = jax.random.normal(key, extent, jnp.float32) * spread
    return jnp.minimum(jnp.maximum(array, -bound), bound).astype(kind)


def setup_inputs(seed: int = 0) -> dict:
    arg_keys = jax.random.split(jax.random.key(seed), 12)
    return {
        "residual_in": draw_residual_in(jax.random.fold_in(arg_keys[11], 71), 0),
        "ritz_vector": draw_ritz_vector(jax.random.fold_in(arg_keys[11], 71), 0),
        "density": jnp.clip(1.0 * jax.random.uniform(arg_keys[2], (NZ, TILES, EY * EX), jnp.float32) ** steps_of(arg_keys[2], (NZ, TILES, EY * EX), ((0, 16), (1, 16)), -0.2, 0.2), 0.0, 1.0),
        "pml_flags": with_ends((jax.random.randint(arg_keys[3], (NZ, TILES, EY * EX), 0, 4) < 1).astype(jnp.int32), jax.random.fold_in(arg_keys[3], 1), 0, 1),
        "design_mask": with_ends((jax.random.randint(arg_keys[4], (NZ, TILES, EY * EX), 0, 2) < 1).astype(jnp.int32), jax.random.fold_in(arg_keys[4], 1), 0, 1),
        "k_base": draw_k_base(jax.random.fold_in(arg_keys[11], 71), 0),
        "k_rho": noise(arg_keys[6], (B, B), B ** -0.5, 0.5, jnp.float32),
        "k_pml": noise(arg_keys[7], (B, B), B ** -0.5, 0.5, jnp.float32),
        "k_face": noise(arg_keys[8], (6, B, B), B ** -0.5, 0.5, jnp.float32),
        "shift_re": jnp.clip(jax.random.uniform(arg_keys[9], (), jnp.float32, 0.5, 2.0), 0.5, 2.0),
        "shift_im": jnp.clip(jax.random.uniform(arg_keys[10], (), jnp.float32, 0.2, 1.0), 0.2, 1.0),
    }


filter_reach = 5

def to_grid(values):
    leading = values.shape[:-3]
    count = len(leading)
    shaped = values.reshape(leading + (NZ, TY, TX, EY, EX))
    shaped = jnp.moveaxis(shaped, count + 3, count + 2)
    return shaped.reshape(leading + (NZ, TY * EY, TX * EX))

def from_grid(values):
    leading = values.shape[:-3]
    count = len(leading)
    shaped = values.reshape(leading + (NZ, TY, EY, TX, EX))
    shaped = jnp.moveaxis(shaped, count + 2, count + 3)
    return shaped.reshape(leading + (NZ, TILES, EY * EX))

def inner_pair(ritz, field):
    half = ritz.shape[0] // 2
    real_part = jnp.sum(ritz[:half] * field[:half] + ritz[half:] * field[half:])
    imag_part = jnp.sum(ritz[:half] * field[half:] - ritz[half:] * field[:half])
    return (real_part, imag_part)

def project_out(field, ritz, coef_re, coef_im):
    half = ritz.shape[0] // 2
    ritz_re = ritz[:half]
    ritz_im = ritz[half:]
    removed = jnp.concatenate([coef_re * ritz_re - coef_im * ritz_im, coef_re * ritz_im + coef_im * ritz_re], axis=0)
    return field - removed

def plane_product(matrix, plane):
    return jnp.einsum('ij,jbc->ibc', matrix, plane, precision=lax.Precision.HIGHEST)

def apply_shifted(field, density, pml_weight, k_base, k_rho, k_pml, k_face, shift_re, shift_im):
    padded = jnp.pad(field, ((0, 0), (1, 1), (1, 1), (1, 1)))
    half = field.shape[0] // 2

    def one_plane(index):
        window = lax.dynamic_slice_in_dim(padded, index, 3, axis=1)
        center = window[:, 1, 1:-1, 1:-1]
        dens_plane = lax.dynamic_index_in_dim(density, index, 0, keepdims=False)
        pml_plane = lax.dynamic_index_in_dim(pml_weight, index, 0, keepdims=False)
        rho_term = plane_product(k_rho, center)
        result = plane_product(k_base, center) + dens_plane * rho_term + pml_plane * plane_product(k_pml, center)
        neighbours = [window[:, 2, 1:-1, 1:-1], window[:, 0, 1:-1, 1:-1], window[:, 1, 2:, 1:-1], window[:, 1, :-2, 1:-1], window[:, 1, 1:-1, 2:], window[:, 1, 1:-1, :-2]]
        for number in range(6):
            result = result + plane_product(k_face[number], neighbours[number])
        real_part = center[:half]
        imag_part = center[half:]
        result = result - jnp.concatenate([shift_re * real_part - shift_im * imag_part, shift_re * imag_part + shift_im * real_part], axis=0)
        return (result, rho_term)
    planes, rho_planes = lax.map(one_plane, jnp.arange(field.shape[1], dtype=jnp.int32))
    return (jnp.moveaxis(planes, 0, 1), jnp.moveaxis(rho_planes, 0, 1))

def smooth_axis(values, axis):
    length = values.shape[axis]
    widths = [(filter_reach, filter_reach) if number == axis else (0, 0) for number in range(3)]
    padded = jnp.pad(values, widths)
    result = jnp.zeros(values.shape, jnp.float32)
    for offset in range(-filter_reach, filter_reach + 1):
        weight = (6.0 - abs(offset)) / 12.0
        result = result + weight * lax.slice_in_dim(padded, filter_reach + offset, filter_reach + offset + length, axis=axis)
    return result

def reference(residual_in, ritz_vector, density, pml_flags, design_mask, k_base, k_rho, k_pml, k_face, shift_re, shift_im):
    residual = to_grid(residual_in)
    ritz = to_grid(ritz_vector)
    dens = to_grid(density)
    pml_weight = to_grid(pml_flags.astype(jnp.float32))
    mask = to_grid(design_mask.astype(jnp.float32))
    ritz_norm = jnp.sum(ritz * ritz)
    first_re, first_im = inner_pair(ritz, residual)
    first = project_out(residual, ritz, first_re / ritz_norm, first_im / ritz_norm)
    image_one, unused = apply_shifted(first, dens, pml_weight, k_base, k_rho, k_pml, k_face, shift_re, shift_im)
    one_re, one_im = inner_pair(ritz, image_one)
    projected = project_out(image_one, ritz, one_re / ritz_norm, one_im / ritz_norm)
    proj_sq = jnp.sum(projected * projected)
    second = projected * jnp.sqrt(B * ELEMS / proj_sq)
    image_two, rho_term = apply_shifted(second, dens, pml_weight, k_base, k_rho, k_pml, k_face, shift_re, shift_im)
    two_re, two_im = inner_pair(ritz, image_two)
    correction = project_out(image_two, ritz, two_re / ritz_norm, two_im / ritz_norm)
    sensitivity = lax.optimization_barrier(jnp.sum(correction * rho_term, axis=0)) / 36.0 * mask
    smoothed = smooth_axis(smooth_axis(smooth_axis(sensitivity, 0), 1), 2)
    return (from_grid(correction), from_grid(smoothed))
```

```python
import jax
import jax.numpy as jnp
from jax import lax
from jax.sharding import Mesh
from jax.sharding import PartitionSpec as P

TX = 4
EY = 8
EX = 16
XY = ("xy_0", "xy_1")
GZ = ("gz_0", "gz_1")


filter_reach = 5


def from_behind(x, axis, by):
    peers = lax.axis_size(axis)
    pairs = [(i, i + by) for i in range(peers) if 0 <= i + by < peers]
    return lax.ppermute(x, axis, pairs)


def with_halo(block, sides, width):
    for axis, dim in sides:
        count = lax.axis_size(axis)
        forward = [(i, i + 1) for i in range(count - 1)]
        backward = [(target, source) for source, target in forward]
        low = lax.ppermute(
            lax.slice_in_dim(block, block.shape[dim] - width, None, axis=dim), axis, forward
        )
        high = lax.ppermute(lax.slice_in_dim(block, 0, width, axis=dim), axis, backward)
        block = jnp.concatenate([low, block, high], axis=dim)
    return block


def from_everyone(x, axis):
    copies = jnp.broadcast_to(x, (lax.axis_size(axis), *x.shape))
    return lax.all_to_all(copies, axis, split_axis=0, concat_axis=0, tiled=True)


def of_everyone(x, axis):
    return from_everyone(x, axis).sum(axis=0)


def by_axis(x, axes):
    far, near = axes
    nearer = of_everyone(x, near)
    return of_everyone(nearer, far)


def in_one(arrays, axis):
    line, at, done = (jnp.concatenate([a.reshape(-1) for a in arrays]), 0, [])
    running = by_axis(line, axis)
    for a in arrays:
        done.append(running[at : at + a.size].reshape(a.shape))
        at += a.size
    return tuple(done)


def inner_pair(ritz, field):
    half = ritz.shape[0] // 2
    real_part = jnp.sum(ritz[:half] * field[:half] + ritz[half:] * field[half:])
    imag_part = jnp.sum(ritz[:half] * field[half:] - ritz[half:] * field[:half])
    return (real_part, imag_part)


def project_out(field, ritz, coef_re, coef_im):
    half = ritz.shape[0] // 2
    ritz_re = ritz[:half]
    ritz_im = ritz[half:]
    removed = jnp.concatenate(
        [coef_re * ritz_re - coef_im * ritz_im, coef_re * ritz_im + coef_im * ritz_re], axis=0
    )
    return field - removed


def lateral(piece, offset):
    return from_behind(piece, XY, offset)


def wide_lateral(piece, offset):
    return from_behind(piece, XY, offset)


def face_rims(field):
    blocks, depth = (field.shape[0], field.shape[1])
    grid = field.reshape(blocks, depth, EY, EX)
    z_deep = with_halo(field, ((GZ, 1),), 1)
    column = lax.axis_index(XY) % TX
    x_minus = jnp.where(column > 0, lateral(grid[:, :, :, EX - 1], 1), 0.0)
    x_plus = jnp.where(column < TX - 1, lateral(grid[:, :, :, 0], -1), 0.0)
    y_minus = lateral(grid[:, :, EY - 1, :], TX)
    y_plus = lateral(grid[:, :, 0, :], -TX)
    return (z_deep, x_minus, x_plus, y_minus, y_plus)


def flatten_cells(values):
    return values.reshape(values.shape[0], values.shape[1], EY * EX)


def assemble(field, rims):
    z_deep, x_minus, x_plus, y_minus, y_plus = rims
    blocks, depth = (field.shape[0], field.shape[1])
    grid = field.reshape(blocks, depth, EY, EX)
    x_padded = jnp.concatenate([x_minus[:, :, :, None], grid, x_plus[:, :, :, None]], axis=3)
    y_padded = jnp.concatenate([y_minus[:, :, None, :], grid, y_plus[:, :, None, :]], axis=2)
    return [
        z_deep[:, 2:],
        z_deep[:, :-2],
        flatten_cells(y_padded[:, :, 2:]),
        flatten_cells(y_padded[:, :, :-2]),
        flatten_cells(x_padded[:, :, :, 2:]),
        flatten_cells(x_padded[:, :, :, :-2]),
    ]


def matrix_apply(matrix, field):
    flat = field.reshape(field.shape[0], -1)
    return jnp.dot(
        matrix, flat, precision=lax.Precision.HIGHEST, preferred_element_type=jnp.float32
    )


def shifted_apply(field, rims, density, pml_weight, k_self, k_face, shift_re, shift_im):
    blocks = field.shape[0]
    half = blocks // 2
    self_terms = matrix_apply(k_self, field).reshape((3,) + field.shape)
    result = self_terms[0] + density * self_terms[1] + pml_weight * self_terms[2]
    neighbours = assemble(field, rims)
    for number in range(6):
        result = result + matrix_apply(k_face[number], neighbours[number]).reshape(field.shape)
    real_part = field[:half]
    imag_part = field[half:]
    result = result - jnp.concatenate(
        [shift_re * real_part - shift_im * imag_part, shift_re * imag_part + shift_im * real_part],
        axis=0,
    )
    return (result, self_terms[1])


def smooth_axis(padded, axis, length):
    result = jnp.zeros(lax.slice_in_dim(padded, 0, length, axis=axis).shape, jnp.float32)
    for offset in range(-filter_reach, filter_reach + 1):
        weight = (6.0 - abs(offset)) / 12.0
        result = result + weight * lax.slice_in_dim(
            padded, filter_reach + offset, filter_reach + offset + length, axis=axis
        )
    return result


ALL = ("gz_0", "gz_1", "xy_0", "xy_1")


def total(values):
    line = jnp.stack(values)
    peers = 1
    for axis in ALL:
        peers *= lax.axis_size(axis)
    copies = jnp.broadcast_to(line, (peers, *line.shape))
    return lax.all_to_all(copies, ALL, split_axis=0, concat_axis=0, tiled=True).sum(axis=0)


def project_rims(rims, ritz_rims, coef_re, coef_im):
    return tuple(project_out(a, b, coef_re, coef_im) for a, b in zip(rims, ritz_rims))


def split_rims(rims, half):
    return (tuple(r[:half] for r in rims), tuple(r[half:] for r in rims))


def smooth_maps(maps, depth):
    deep = with_halo(maps, ((GZ, 1),), filter_reach)
    smooth_z = smooth_axis(deep, 1, depth).reshape(maps.shape[0], depth, EY, EX)
    column = lax.axis_index(XY) % TX
    below = wide_lateral(smooth_z[:, :, EY - filter_reach :, :], TX)
    above = wide_lateral(smooth_z[:, :, :filter_reach, :], -TX)
    smooth_y = smooth_axis(jnp.concatenate([below, smooth_z, above], axis=2), 2, EY)
    left_part = jnp.where(column > 0, wide_lateral(smooth_y[:, :, :, EX - filter_reach :], 1), 0.0)
    right_part = jnp.where(column < TX - 1, wide_lateral(smooth_y[:, :, :, :filter_reach], -1), 0.0)
    smooth_x = smooth_axis(jnp.concatenate([left_part, smooth_y, right_part], axis=3), 3, EX)
    return smooth_x.reshape(maps.shape[0], depth, EY * EX)


def local(
    residual_in,
    ritz_vector,
    density,
    pml_flags,
    design_mask,
    k_base,
    k_rho,
    k_pml,
    k_face,
    shift_re,
    shift_im,
):
    residual = residual_in[:, :, 0, :]
    ritz = ritz_vector[:, :, 0, :]
    dens = density[:, 0, :]
    pml_weight = pml_flags[:, 0, :].astype(jnp.float32)
    mask = design_mask[:, 0, :].astype(jnp.float32)
    k_self = jnp.concatenate([k_base, k_rho, k_pml], axis=0)
    blocks, depth, cells = residual.shape
    half = blocks // 2
    count = blocks * depth * cells * lax.axis_size(GZ) * lax.axis_size(XY)
    first_re, first_im = inner_pair(ritz, residual)
    ritz_norm, first_re, first_im = total((jnp.sum(ritz * ritz), first_re, first_im))
    both_rims = face_rims(jnp.concatenate([residual, ritz], axis=0))
    res_rims, ritz_rims = split_rims(both_rims, blocks)
    coef_re = first_re / ritz_norm
    coef_im = first_im / ritz_norm
    first = project_out(residual, ritz, coef_re, coef_im)
    first_rims = project_rims(res_rims, ritz_rims, coef_re, coef_im)
    image_one, unused = shifted_apply(
        first, first_rims, dens, pml_weight, k_self, k_face, shift_re, shift_im
    )
    one_re, one_im = inner_pair(ritz, image_one)
    one_re, one_im, image_sq = total((one_re, one_im, jnp.sum(image_one * image_one)))
    image_rims = face_rims(image_one)
    two_coef_re = one_re / ritz_norm
    two_coef_im = one_im / ritz_norm
    projected = project_out(image_one, ritz, two_coef_re, two_coef_im)
    proj_rims = project_rims(image_rims, ritz_rims, two_coef_re, two_coef_im)
    proj_sq = image_sq - (one_re * one_re + one_im * one_im) / ritz_norm
    factor = jnp.sqrt(count / proj_sq)
    image_two, rho_term = shifted_apply(
        projected, proj_rims, dens, pml_weight, k_self, k_face, shift_re, shift_im
    )
    two_re, two_im = inner_pair(ritz, image_two)
    two_re, two_im = total((two_re, two_im))
    ritz_re = ritz[:half]
    ritz_im = ritz[half:]
    rho_re = rho_term[:half]
    rho_im = rho_term[half:]
    maps = jnp.stack(
        [
            jnp.sum(image_two * rho_term, axis=0),
            jnp.sum(ritz_re * rho_re + ritz_im * rho_im, axis=0),
            jnp.sum(ritz_re * rho_im - ritz_im * rho_re, axis=0),
        ]
    ) * mask
    smoothed = smooth_maps(maps, depth)
    three_re = two_re / ritz_norm
    three_im = two_im / ritz_norm
    correction = project_out(image_two, ritz, three_re, three_im) * factor
    scale = factor * factor / 36.0
    filtered = (smoothed[0] - three_re * smoothed[1] - three_im * smoothed[2]) * scale
    return (correction[:, :, None, :], filtered.reshape(depth, 1, EY * EX))


def solution(mesh):
    torus = Mesh(mesh.devices.reshape(4, 4, 8, 2), ("gz_0", "gz_1", "xy_0", "xy_1"))
    placed = (
        P(None, GZ, XY, None),
        P(None, GZ, XY, None),
        P(GZ, XY, None),
        P(GZ, XY, None),
        P(GZ, XY, None),
        P(),
        P(),
        P(),
        P(),
        P(),
        P(),
    )
    return jax.shard_map(
        local,
        mesh=torus,
        in_specs=placed,
        out_specs=(P(None, GZ, XY, None), P(GZ, XY, None)),
        check_vma=False,
    )
```

```python
import jax
import jax.numpy as jnp
from jax import lax
from jax.sharding import Mesh
from jax.sharding import PartitionSpec as P

TX = 4
EY = 8
EX = 16
XY = ("xy_0", "xy_1")
GZ = ("gz_0", "gz_1")


filter_reach = 5


def from_behind(x, axis, by):
    peers = lax.axis_size(axis)
    pairs = [(i, i + by) for i in range(peers) if 0 <= i + by < peers]
    return lax.ppermute(x, axis, pairs)


def with_halo(block, sides, width):
    for axis, dim in sides:
        count = lax.axis_size(axis)
        forward = [(i, i + 1) for i in range(count - 1)]
        backward = [(target, source) for source, target in forward]
        low = lax.ppermute(
            lax.slice_in_dim(block, block.shape[dim] - width, None, axis=dim), axis, forward
        )
        high = lax.ppermute(lax.slice_in_dim(block, 0, width, axis=dim), axis, backward)
        block = jnp.concatenate([low, block, high], axis=dim)
    return block


def from_everyone(x, axis):
    copies = jnp.broadcast_to(x, (lax.axis_size(axis), *x.shape))
    return lax.all_to_all(copies, axis, split_axis=0, concat_axis=0, tiled=True)


def of_everyone(x, axis):
    return from_everyone(x, axis).sum(axis=0)


def by_axis(x, axes):
    far, near = axes
    nearer = of_everyone(x, near)
    return of_everyone(nearer, far)


def in_one(arrays, axis):
    line, at, done = (jnp.concatenate([a.reshape(-1) for a in arrays]), 0, [])
    running = by_axis(line, axis)
    for a in arrays:
        done.append(running[at : at + a.size].reshape(a.shape))
        at += a.size
    return tuple(done)


def inner_pair(ritz, field):
    half = ritz.shape[0] // 2
    real_part = jnp.sum(ritz[:half] * field[:half] + ritz[half:] * field[half:])
    imag_part = jnp.sum(ritz[:half] * field[half:] - ritz[half:] * field[:half])
    return (real_part, imag_part)


def project_out(field, ritz, coef_re, coef_im):
    half = ritz.shape[0] // 2
    ritz_re = ritz[:half]
    ritz_im = ritz[half:]
    removed = jnp.concatenate(
        [coef_re * ritz_re - coef_im * ritz_im, coef_re * ritz_im + coef_im * ritz_re], axis=0
    )
    return field - removed


def lateral(piece, offset):
    return from_behind(piece, XY, offset)


def wide_lateral(piece, offset):
    return from_behind(piece, XY, offset)


def face_rims(field):
    blocks, depth = (field.shape[0], field.shape[1])
    grid = field.reshape(blocks, depth, EY, EX)
    z_deep = with_halo(field, ((GZ, 1),), 1)
    column = lax.axis_index(XY) % TX
    x_minus = jnp.where(column > 0, lateral(grid[:, :, :, EX - 1], 1), 0.0)
    x_plus = jnp.where(column < TX - 1, lateral(grid[:, :, :, 0], -1), 0.0)
    y_minus = lateral(grid[:, :, EY - 1, :], TX)
    y_plus = lateral(grid[:, :, 0, :], -TX)
    return (z_deep, x_minus, x_plus, y_minus, y_plus)


def flatten_cells(values):
    return values.reshape(values.shape[0], values.shape[1], EY * EX)


def assemble(field, rims):
    z_deep, x_minus, x_plus, y_minus, y_plus = rims
    blocks, depth = (field.shape[0], field.shape[1])
    grid = field.reshape(blocks, depth, EY, EX)
    x_padded = jnp.concatenate([x_minus[:, :, :, None], grid, x_plus[:, :, :, None]], axis=3)
    y_padded = jnp.concatenate([y_minus[:, :, None, :], grid, y_plus[:, :, None, :]], axis=2)
    return [
        z_deep[:, 2:],
        z_deep[:, :-2],
        flatten_cells(y_padded[:, :, 2:]),
        flatten_cells(y_padded[:, :, :-2]),
        flatten_cells(x_padded[:, :, :, 2:]),
        flatten_cells(x_padded[:, :, :, :-2]),
    ]


def matrix_apply(matrix, field):
    flat = field.reshape(field.shape[0], -1)
    return jnp.dot(
        matrix, flat, precision=lax.Precision.HIGHEST, preferred_element_type=jnp.float32
    )


def shifted_apply(field, rims, density, pml_weight, k_self, k_face, shift_re, shift_im):
    blocks = field.shape[0]
    half = blocks // 2
    self_terms = matrix_apply(k_self, field).reshape((3,) + field.shape)
    result = self_terms[0] + density * self_terms[1] + pml_weight * self_terms[2]
    neighbours = assemble(field, rims)
    for number in range(6):
        result = result + matrix_apply(k_face[number], neighbours[number]).reshape(field.shape)
    real_part = field[:half]
    imag_part = field[half:]
    result = result - jnp.concatenate(
        [shift_re * real_part - shift_im * imag_part, shift_re * imag_part + shift_im * real_part],
        axis=0,
    )
    return (result, self_terms[1])


def smooth_axis(padded, axis, length):
    result = jnp.zeros(lax.slice_in_dim(padded, 0, length, axis=axis).shape, jnp.float32)
    for offset in range(-filter_reach, filter_reach + 1):
        weight = (6.0 - abs(offset)) / 12.0
        result = result + weight * lax.slice_in_dim(
            padded, filter_reach + offset, filter_reach + offset + length, axis=axis
        )
    return result


ALL = ("gz_0", "gz_1", "xy_0", "xy_1")


def total(line):
    peers = 1
    for axis in ALL:
        peers *= lax.axis_size(axis)
    copies = jnp.broadcast_to(line, (peers, *line.shape))
    return lax.all_to_all(copies, ALL, split_axis=0, concat_axis=0, tiled=True).sum(axis=0)


def turned(piece):
    half = piece.shape[0] // 2
    return jnp.concatenate([-piece[half:], piece[:half]], axis=0)


def exchange(stack):
    channels, fields, depth, cells = stack.shape
    grid = stack.reshape(channels, fields, depth, EY, EX)
    column = lax.axis_index(XY) % TX
    z_low = from_behind(stack[:, :, depth - 1 :], GZ, 1)
    z_high = from_behind(stack[:, :, :1], GZ, -1)
    x_minus = jnp.where(column > 0, lateral(grid[..., EX - 1], 1), 0.0)
    x_plus = jnp.where(column < TX - 1, lateral(grid[..., 0], -1), 0.0)
    y_minus = lateral(grid[:, :, :, EY - 1, :], TX)
    y_plus = lateral(grid[:, :, :, 0, :], -TX)
    return (z_low, z_high, x_minus, x_plus, y_minus, y_plus)


def neighbour_terms(stack, rims):
    z_low, z_high, x_minus, x_plus, y_minus, y_plus = rims
    channels, fields, depth, cells = stack.shape
    grid = stack.reshape(channels, fields, depth, EY, EX)
    deep = jnp.concatenate([z_low, stack, z_high], axis=2)
    y_padded = jnp.concatenate([y_minus[:, :, :, None, :], grid, y_plus[:, :, :, None, :]], axis=3)
    x_padded = jnp.concatenate([x_minus[..., None], grid, x_plus[..., None]], axis=4)
    return [
        deep[:, :, 2:],
        deep[:, :, :-2],
        y_padded[:, :, :, 2:],
        y_padded[:, :, :, :-2],
        x_padded[..., 2:],
        x_padded[..., :-2],
    ]


def level_apply(stack, rims, dens, pml_weight, k_all):
    channels, fields, depth, cells = stack.shape
    terms = [stack, stack * dens, stack * pml_weight] + neighbour_terms(stack, rims)
    rhs = jnp.concatenate([t.reshape(channels, -1) for t in terms], axis=0)
    out = jnp.dot(k_all, rhs, precision=lax.Precision.HIGH, preferred_element_type=jnp.float32)
    return out.reshape(channels, fields, depth, cells)


def local(
    residual_in,
    ritz_vector,
    density,
    pml_flags,
    design_mask,
    k_base,
    k_rho,
    k_pml,
    k_face,
    shift_re,
    shift_im,
):
    residual = residual_in[:, :, 0, :]
    ritz = ritz_vector[:, :, 0, :]
    dens = density[:, 0, :]
    pml_weight = pml_flags[:, 0, :].astype(jnp.float32)
    mask = design_mask[:, 0, :].astype(jnp.float32)
    blocks, depth, cells = residual.shape
    half = blocks // 2
    count = blocks * depth * cells * lax.axis_size(GZ) * lax.axis_size(XY)
    eye = jnp.eye(half, dtype=jnp.float32)
    sigma = jnp.block([[shift_re * eye, -shift_im * eye], [shift_im * eye, shift_re * eye]])
    k_all = jnp.concatenate([k_base - sigma, k_rho, k_pml] + [k_face[n] for n in range(6)], axis=1)
    ritz_turned = turned(ritz)
    pair = jnp.stack([residual, ritz], axis=1)
    pair_rims = exchange(pair)
    first_re, first_im = inner_pair(ritz, residual)
    g_one = total(jnp.stack([jnp.sum(ritz * ritz), first_re, first_im]))
    rims_one = tuple(jnp.concatenate([p, turned(p[:, 1:2])], axis=1) for p in pair_rims)
    level_in = jnp.concatenate([pair, ritz_turned[:, None]], axis=1)
    level_one = level_apply(level_in, rims_one, dens, pml_weight, k_all)
    ritz_norm = g_one[0]
    c1_re = g_one[1] / ritz_norm
    c1_im = g_one[2] / ritz_norm
    a1, b1, cc1 = level_one[:, 0], level_one[:, 1], level_one[:, 2]
    image_one = a1 - c1_re * b1 - c1_im * cc1
    image_rims = exchange(image_one[:, None])
    image_s = level_apply(image_one[:, None], image_rims, dens, pml_weight, k_all)[:, 0]
    left = jnp.stack([ritz, ritz_turned], axis=1)
    right = jnp.stack([image_one, image_s, b1, cc1], axis=1)
    gram = lax.dot_general(
        left,
        right,
        (((0, 2, 3), (0, 2, 3)), ((), ())),
        precision=lax.Precision.HIGHEST,
        preferred_element_type=jnp.float32,
    )
    g = total(jnp.concatenate([gram.reshape(-1), jnp.sum(image_one * image_one)[None]]))
    g = g[:8].reshape(2, 4), g[8]
    g, image_sq = g
    one_re, one_im = g[0, 0], g[1, 0]
    c2_re = one_re / ritz_norm
    c2_im = one_im / ritz_norm
    proj_sq = image_sq - (one_re * one_re + one_im * one_im) / ritz_norm
    factor = jnp.sqrt(count / proj_sq)
    t_re = g[0, 1] - c2_re * g[0, 2] - c2_im * g[0, 3]
    t_im = g[1, 1] - c2_re * g[1, 2] - c2_im * g[1, 3]
    c3_re = t_re / ritz_norm
    c3_im = t_im / ritz_norm
    image_two = image_s - c2_re * b1 - c2_im * cc1
    projected = image_one - c2_re * ritz - c2_im * ritz_turned
    correction = (image_two - c3_re * ritz - c3_im * ritz_turned) * factor
    rho_term = matrix_apply(k_rho, projected * factor).reshape(projected.shape)
    sensitivity = jnp.sum(correction * rho_term, axis=0) / 36.0 * mask
    deep_sens = with_halo(sensitivity, ((GZ, 0),), filter_reach)
    smooth_z = smooth_axis(deep_sens, 0, depth).reshape(depth, EY, EX)
    column = lax.axis_index(XY) % TX
    below = wide_lateral(smooth_z[:, EY - filter_reach :, :], TX)
    above = wide_lateral(smooth_z[:, :filter_reach, :], -TX)
    smooth_y = smooth_axis(jnp.concatenate([below, smooth_z, above], axis=1), 1, EY)
    left_part = jnp.where(column > 0, wide_lateral(smooth_y[:, :, EX - filter_reach :], 1), 0.0)
    right_part = jnp.where(column < TX - 1, wide_lateral(smooth_y[:, :, :filter_reach], -1), 0.0)
    smooth_x = smooth_axis(jnp.concatenate([left_part, smooth_y, right_part], axis=2), 2, EX)
    filtered = smooth_x.reshape(depth, 1, EY * EX)
    return (correction[:, :, None, :], filtered)


def solution(mesh):
    torus = Mesh(mesh.devices.reshape(4, 4, 8, 2), ("gz_0", "gz_1", "xy_0", "xy_1"))
    placed = (
        P(None, GZ, XY, None),
        P(None, GZ, XY, None),
        P(GZ, XY, None),
        P(GZ, XY, None),
        P(GZ, XY, None),
        P(),
        P(),
        P(),
        P(),
        P(),
        P(),
    )
    return jax.shard_map(
        local,
        mesh=torus,
        in_specs=placed,
        out_specs=(P(None, GZ, XY, None), P(GZ, XY, None)),
        check_vma=False,
    )
```

```python
import jax
import jax.numpy as jnp
from jax import lax
from jax.sharding import Mesh
from jax.sharding import PartitionSpec as P

TX = 4
EY = 8
EX = 16
XY = ("xy_0", "xy_1")
GZ = ("gz_0", "gz_1")


filter_reach = 5


def from_behind(x, axis, by):
    peers = lax.axis_size(axis)
    pairs = [(i, i + by) for i in range(peers) if 0 <= i + by < peers]
    return lax.ppermute(x, axis, pairs)


def with_halo(block, sides, width):
    for axis, dim in sides:
        count = lax.axis_size(axis)
        forward = [(i, i + 1) for i in range(count - 1)]
        backward = [(target, source) for source, target in forward]
        low = lax.ppermute(
            lax.slice_in_dim(block, block.shape[dim] - width, None, axis=dim), axis, forward
        )
        high = lax.ppermute(lax.slice_in_dim(block, 0, width, axis=dim), axis, backward)
        block = jnp.concatenate([low, block, high], axis=dim)
    return block


def from_everyone(x, axis):
    copies = jnp.broadcast_to(x, (lax.axis_size(axis), *x.shape))
    return lax.all_to_all(copies, axis, split_axis=0, concat_axis=0, tiled=True)


def of_everyone(x, axis):
    return from_everyone(x, axis).sum(axis=0)


def by_axis(x, axes):
    far, near = axes
    nearer = of_everyone(x, near)
    return of_everyone(nearer, far)


def in_one(arrays, axis):
    line, at, done = (jnp.concatenate([a.reshape(-1) for a in arrays]), 0, [])
    running = by_axis(line, axis)
    for a in arrays:
        done.append(running[at : at + a.size].reshape(a.shape))
        at += a.size
    return tuple(done)


def inner_pair(ritz, field):
    half = ritz.shape[0] // 2
    real_part = jnp.sum(ritz[:half] * field[:half] + ritz[half:] * field[half:])
    imag_part = jnp.sum(ritz[:half] * field[half:] - ritz[half:] * field[:half])
    return (real_part, imag_part)


def project_out(field, ritz, coef_re, coef_im):
    half = ritz.shape[0] // 2
    ritz_re = ritz[:half]
    ritz_im = ritz[half:]
    removed = jnp.concatenate(
        [coef_re * ritz_re - coef_im * ritz_im, coef_re * ritz_im + coef_im * ritz_re], axis=0
    )
    return field - removed


def lateral(piece, offset):
    return from_behind(piece, XY, offset)


def wide_lateral(piece, offset):
    return from_behind(piece, XY, offset)


def face_rims(field):
    blocks, depth = (field.shape[0], field.shape[1])
    grid = field.reshape(blocks, depth, EY, EX)
    z_deep = with_halo(field, ((GZ, 1),), 1)
    column = lax.axis_index(XY) % TX
    x_minus = jnp.where(column > 0, lateral(grid[:, :, :, EX - 1], 1), 0.0)
    x_plus = jnp.where(column < TX - 1, lateral(grid[:, :, :, 0], -1), 0.0)
    y_minus = lateral(grid[:, :, EY - 1, :], TX)
    y_plus = lateral(grid[:, :, 0, :], -TX)
    return (z_deep, x_minus, x_plus, y_minus, y_plus)


def flatten_cells(values):
    return values.reshape(values.shape[0], values.shape[1], EY * EX)


def assemble(field, rims):
    z_deep, x_minus, x_plus, y_minus, y_plus = rims
    blocks, depth = (field.shape[0], field.shape[1])
    grid = field.reshape(blocks, depth, EY, EX)
    x_padded = jnp.concatenate([x_minus[:, :, :, None], grid, x_plus[:, :, :, None]], axis=3)
    y_padded = jnp.concatenate([y_minus[:, :, None, :], grid, y_plus[:, :, None, :]], axis=2)
    return [
        z_deep[:, 2:],
        z_deep[:, :-2],
        flatten_cells(y_padded[:, :, 2:]),
        flatten_cells(y_padded[:, :, :-2]),
        flatten_cells(x_padded[:, :, :, 2:]),
        flatten_cells(x_padded[:, :, :, :-2]),
    ]


def matrix_apply(matrix, field):
    flat = field.reshape(field.shape[0], -1)
    return jnp.dot(
        matrix, flat, precision=lax.Precision.HIGHEST, preferred_element_type=jnp.float32
    )


def shifted_apply(field, rims, density, pml_weight, k_self, k_face, shift_re, shift_im):
    blocks = field.shape[0]
    half = blocks // 2
    self_terms = matrix_apply(k_self, field).reshape((3,) + field.shape)
    result = self_terms[0] + density * self_terms[1] + pml_weight * self_terms[2]
    neighbours = assemble(field, rims)
    for number in range(6):
        result = result + matrix_apply(k_face[number], neighbours[number]).reshape(field.shape)
    real_part = field[:half]
    imag_part = field[half:]
    result = result - jnp.concatenate(
        [shift_re * real_part - shift_im * imag_part, shift_re * imag_part + shift_im * real_part],
        axis=0,
    )
    return (result, self_terms[1])


def smooth_axis(padded, axis, length):
    result = jnp.zeros(lax.slice_in_dim(padded, 0, length, axis=axis).shape, jnp.float32)
    for offset in range(-filter_reach, filter_reach + 1):
        weight = (6.0 - abs(offset)) / 12.0
        result = result + weight * lax.slice_in_dim(
            padded, filter_reach + offset, filter_reach + offset + length, axis=axis
        )
    return result


ALL = ("gz_0", "gz_1", "xy_0", "xy_1")


def total(line):
    peers = 1
    for axis in ALL:
        peers *= lax.axis_size(axis)
    copies = jnp.broadcast_to(line, (peers, *line.shape))
    return lax.all_to_all(copies, ALL, split_axis=0, concat_axis=0, tiled=True).sum(axis=0)


def turned(piece):
    half = piece.shape[0] // 2
    return jnp.concatenate([-piece[half:], piece[:half]], axis=0)


def exchange(stack):
    channels, fields, depth, cells = stack.shape
    column = lax.axis_index(XY) % TX
    z_low = from_behind(stack[:, :, depth - 1 :], GZ, 1)
    z_high = from_behind(stack[:, :, :1], GZ, -1)
    x_minus = jnp.where(column > 0, lateral(stack[..., EX - 1 :: EX], 1), 0.0)
    x_plus = jnp.where(column < TX - 1, lateral(stack[..., ::EX], -1), 0.0)
    y_minus = lateral(stack[..., cells - EX :], TX)
    y_plus = lateral(stack[..., :EX], -TX)
    return (z_low, z_high, x_minus, x_plus, y_minus, y_plus)


def neighbour_terms(stack, rims):
    z_low, z_high, x_minus, x_plus, y_minus, y_plus = rims
    lane = jnp.arange(stack.shape[-1]) % EX
    deep = jnp.concatenate([z_low, stack, z_high], axis=2)
    zero = jnp.zeros(stack.shape[:-1] + (1,), jnp.float32)
    x_next = jnp.concatenate([stack[..., 1:], zero], axis=-1)
    x_prev = jnp.concatenate([zero, stack[..., :-1]], axis=-1)
    return [
        deep[:, :, 2:],
        deep[:, :, :-2],
        jnp.concatenate([stack[..., EX:], y_plus], axis=-1),
        jnp.concatenate([y_minus, stack[..., :-EX]], axis=-1),
        jnp.where(lane == EX - 1, jnp.repeat(x_plus, EX, axis=-1), x_next),
        jnp.where(lane == 0, jnp.repeat(x_minus, EX, axis=-1), x_prev),
    ]


def level_apply(stack, rims, dens, pml_weight, k_all):
    channels, fields, depth, cells = stack.shape
    terms = [stack, stack * dens, stack * pml_weight] + neighbour_terms(stack, rims)
    rhs = jnp.concatenate([t.reshape(channels, -1) for t in terms], axis=0)
    out = jnp.dot(k_all, rhs, precision=lax.Precision.HIGHEST, preferred_element_type=jnp.float32)
    return out.reshape(channels, fields, depth, cells)


def local(
    residual_in,
    ritz_vector,
    density,
    pml_flags,
    design_mask,
    k_base,
    k_rho,
    k_pml,
    k_face,
    shift_re,
    shift_im,
):
    residual = residual_in[:, :, 0, :]
    ritz = ritz_vector[:, :, 0, :]
    dens = density[:, 0, :]
    pml_weight = pml_flags[:, 0, :].astype(jnp.float32)
    mask = design_mask[:, 0, :].astype(jnp.float32)
    blocks, depth, cells = residual.shape
    half = blocks // 2
    count = blocks * depth * cells * lax.axis_size(GZ) * lax.axis_size(XY)
    eye = jnp.eye(half, dtype=jnp.float32)
    sigma = jnp.block([[shift_re * eye, -shift_im * eye], [shift_im * eye, shift_re * eye]])
    k_all = jnp.concatenate([k_base - sigma, k_rho, k_pml] + [k_face[n] for n in range(6)], axis=1)
    ritz_turned = turned(ritz)
    pair = jnp.stack([residual, ritz], axis=1)
    pair_rims = exchange(pair)
    first_re, first_im = inner_pair(ritz, residual)
    g_one = total(jnp.stack([jnp.sum(ritz * ritz), first_re, first_im]))
    rims_one = tuple(jnp.concatenate([p, turned(p[:, 1:2])], axis=1) for p in pair_rims)
    level_in = jnp.concatenate([pair, ritz_turned[:, None]], axis=1)
    level_one = level_apply(level_in, rims_one, dens, pml_weight, k_all)
    ritz_norm = g_one[0]
    c1_re = g_one[1] / ritz_norm
    c1_im = g_one[2] / ritz_norm
    a1, b1, cc1 = level_one[:, 0], level_one[:, 1], level_one[:, 2]
    image_one = a1 - c1_re * b1 - c1_im * cc1
    image_rims = exchange(image_one[:, None])
    image_s = level_apply(image_one[:, None], image_rims, dens, pml_weight, k_all)[:, 0]
    sums = [jnp.sum(image_one * image_one)]
    for field in (image_one, image_s, b1, cc1):
        sums += [jnp.sum(ritz * field), jnp.sum(ritz_turned * field)]
    g = total(jnp.stack(sums))
    image_sq = g[0]
    g = g[1:].reshape(4, 2).T
    one_re, one_im = g[0, 0], g[1, 0]
    c2_re = one_re / ritz_norm
    c2_im = one_im / ritz_norm
    proj_sq = image_sq - (one_re * one_re + one_im * one_im) / ritz_norm
    factor = jnp.sqrt(count / proj_sq)
    t_re = g[0, 1] - c2_re * g[0, 2] - c2_im * g[0, 3]
    t_im = g[1, 1] - c2_re * g[1, 2] - c2_im * g[1, 3]
    c3_re = t_re / ritz_norm
    c3_im = t_im / ritz_norm
    image_two = image_s - c2_re * b1 - c2_im * cc1
    projected = image_one - c2_re * ritz - c2_im * ritz_turned
    correction = (image_two - c3_re * ritz - c3_im * ritz_turned) * factor
    rho_term = matrix_apply(k_rho, projected * factor).reshape(projected.shape)
    sensitivity = jnp.sum(correction * rho_term, axis=0) / 36.0 * mask
    deep_sens = with_halo(sensitivity, ((GZ, 0),), filter_reach)
    smooth_z = smooth_axis(deep_sens, 0, depth).reshape(depth, EY, EX)
    column = lax.axis_index(XY) % TX
    below = wide_lateral(smooth_z[:, EY - filter_reach :, :], TX)
    above = wide_lateral(smooth_z[:, :filter_reach, :], -TX)
    smooth_y = smooth_axis(jnp.concatenate([below, smooth_z, above], axis=1), 1, EY)
    left_part = jnp.where(column > 0, wide_lateral(smooth_y[:, :, EX - filter_reach :], 1), 0.0)
    right_part = jnp.where(column < TX - 1, wide_lateral(smooth_y[:, :, :filter_reach], -1), 0.0)
    smooth_x = smooth_axis(jnp.concatenate([left_part, smooth_y, right_part], axis=2), 2, EX)
    filtered = smooth_x.reshape(depth, 1, EY * EX)
    return (correction[:, :, None, :], filtered)


def solution(mesh):
    torus = Mesh(mesh.devices.reshape(4, 4, 8, 2), ("gz_0", "gz_1", "xy_0", "xy_1"))
    placed = (
        P(None, GZ, XY, None),
        P(None, GZ, XY, None),
        P(GZ, XY, None),
        P(GZ, XY, None),
        P(GZ, XY, None),
        P(),
        P(),
        P(),
        P(),
        P(),
        P(),
    )
    return jax.shard_map(
        local,
        mesh=torus,
        in_specs=placed,
        out_specs=(P(None, GZ, XY, None), P(GZ, XY, None)),
        check_vma=False,
    )
```

```python
import jax
import jax.numpy as jnp
from jax import lax
from jax.sharding import Mesh
from jax.sharding import PartitionSpec as P

TX = 4
EY = 8
EX = 16
XY = ("xy_0", "xy_1")
GZ = ("gz_0", "gz_1")


filter_reach = 5


def from_behind(x, axis, by):
    peers = lax.axis_size(axis)
    pairs = [(i, i + by) for i in range(peers) if 0 <= i + by < peers]
    return lax.ppermute(x, axis, pairs)


def with_halo(block, sides, width):
    for axis, dim in sides:
        count = lax.axis_size(axis)
        forward = [(i, i + 1) for i in range(count - 1)]
        backward = [(target, source) for source, target in forward]
        low = lax.ppermute(
            lax.slice_in_dim(block, block.shape[dim] - width, None, axis=dim), axis, forward
        )
        high = lax.ppermute(lax.slice_in_dim(block, 0, width, axis=dim), axis, backward)
        block = jnp.concatenate([low, block, high], axis=dim)
    return block


def from_everyone(x, axis):
    copies = jnp.broadcast_to(x, (lax.axis_size(axis), *x.shape))
    return lax.all_to_all(copies, axis, split_axis=0, concat_axis=0, tiled=True)


def of_everyone(x, axis):
    return from_everyone(x, axis).sum(axis=0)


def by_axis(x, axes):
    far, near = axes
    nearer = of_everyone(x, near)
    return of_everyone(nearer, far)


def in_one(arrays, axis):
    line, at, done = (jnp.concatenate([a.reshape(-1) for a in arrays]), 0, [])
    running = by_axis(line, axis)
    for a in arrays:
        done.append(running[at : at + a.size].reshape(a.shape))
        at += a.size
    return tuple(done)


def inner_pair(ritz, field):
    half = ritz.shape[0] // 2
    real_part = jnp.sum(ritz[:half] * field[:half] + ritz[half:] * field[half:])
    imag_part = jnp.sum(ritz[:half] * field[half:] - ritz[half:] * field[:half])
    return (real_part, imag_part)


def project_out(field, ritz, coef_re, coef_im):
    half = ritz.shape[0] // 2
    ritz_re = ritz[:half]
    ritz_im = ritz[half:]
    removed = jnp.concatenate(
        [coef_re * ritz_re - coef_im * ritz_im, coef_re * ritz_im + coef_im * ritz_re], axis=0
    )
    return field - removed


def lateral(piece, offset):
    return from_behind(piece, XY, offset)


def wide_lateral(piece, offset):
    return from_behind(piece, XY, offset)


def face_rims(field):
    blocks, depth, cells = field.shape
    z_deep = with_halo(field, ((GZ, 1),), 1)
    column = lax.axis_index(XY) % TX
    x_minus = jnp.where(column > 0, lateral(field[:, :, EX - 1 :: EX], 1), 0.0)
    x_plus = jnp.where(column < TX - 1, lateral(field[:, :, ::EX], -1), 0.0)
    y_minus = lateral(field[:, :, cells - EX :], TX)
    y_plus = lateral(field[:, :, :EX], -TX)
    return (z_deep, x_minus, x_plus, y_minus, y_plus)


def assemble(field, rims):
    z_deep, x_minus, x_plus, y_minus, y_plus = rims
    lane = jnp.arange(field.shape[-1]) % EX
    zero = jnp.zeros(field.shape[:-1] + (1,), jnp.float32)
    x_next = jnp.concatenate([field[..., 1:], zero], axis=-1)
    x_prev = jnp.concatenate([zero, field[..., :-1]], axis=-1)
    return [
        z_deep[:, 2:],
        z_deep[:, :-2],
        jnp.concatenate([field[..., EX:], y_plus], axis=-1),
        jnp.concatenate([y_minus, field[..., :-EX]], axis=-1),
        jnp.where(lane == EX - 1, jnp.repeat(x_plus, EX, axis=-1), x_next),
        jnp.where(lane == 0, jnp.repeat(x_minus, EX, axis=-1), x_prev),
    ]


def matrix_apply(matrix, field):
    flat = field.reshape(field.shape[0], -1)
    return jnp.dot(
        matrix, flat, precision=lax.Precision.HIGHEST, preferred_element_type=jnp.float32
    )


def shifted_apply(field, rims, density, pml_weight, k_self, k_face, shift_re, shift_im):
    blocks = field.shape[0]
    half = blocks // 2
    self_terms = matrix_apply(k_self, field).reshape((3,) + field.shape)
    result = self_terms[0] + density * self_terms[1] + pml_weight * self_terms[2]
    neighbours = assemble(field, rims)
    for number in range(6):
        result = result + matrix_apply(k_face[number], neighbours[number]).reshape(field.shape)
    real_part = field[:half]
    imag_part = field[half:]
    result = result - jnp.concatenate(
        [shift_re * real_part - shift_im * imag_part, shift_re * imag_part + shift_im * real_part],
        axis=0,
    )
    return (result, self_terms[1])


def smooth_axis(padded, axis, length):
    result = jnp.zeros(lax.slice_in_dim(padded, 0, length, axis=axis).shape, jnp.float32)
    for offset in range(-filter_reach, filter_reach + 1):
        weight = (6.0 - abs(offset)) / 12.0
        result = result + weight * lax.slice_in_dim(
            padded, filter_reach + offset, filter_reach + offset + length, axis=axis
        )
    return result


def local(
    residual_in,
    ritz_vector,
    density,
    pml_flags,
    design_mask,
    k_base,
    k_rho,
    k_pml,
    k_face,
    shift_re,
    shift_im,
):
    residual = residual_in[:, :, 0, :]
    ritz = ritz_vector[:, :, 0, :]
    dens = density[:, 0, :]
    pml_weight = pml_flags[:, 0, :].astype(jnp.float32)
    mask = design_mask[:, 0, :].astype(jnp.float32)
    k_self = jnp.concatenate([k_base, k_rho, k_pml], axis=0)
    blocks, depth, cells = residual.shape
    count = blocks * depth * cells * lax.axis_size(GZ) * lax.axis_size(XY)
    first_re, first_im = inner_pair(ritz, residual)
    ritz_norm, first_re, first_im = in_one(
        (jnp.sum(ritz * ritz), first_re, first_im), ("gz_0", ("gz_1", "xy_0", "xy_1"))
    )
    coef_re = first_re / ritz_norm
    coef_im = first_im / ritz_norm
    first = project_out(residual, ritz, coef_re, coef_im)
    first_rims = face_rims(first)
    image_one, unused = shifted_apply(
        first, first_rims, dens, pml_weight, k_self, k_face, shift_re, shift_im
    )
    one_re, one_im = inner_pair(ritz, image_one)
    one_re, one_im, image_sq = in_one(
        (one_re, one_im, jnp.sum(image_one * image_one)), ("gz_0", ("gz_1", "xy_0", "xy_1"))
    )
    projected = project_out(image_one, ritz, one_re / ritz_norm, one_im / ritz_norm)
    proj_sq = image_sq - (one_re * one_re + one_im * one_im) / ritz_norm
    factor = jnp.sqrt(count / proj_sq)
    second = projected * factor
    second_rims = face_rims(second)
    image_two, rho_term = shifted_apply(
        second, second_rims, dens, pml_weight, k_self, k_face, shift_re, shift_im
    )
    two_re, two_im = inner_pair(ritz, image_two)
    two_re, two_im = in_one((two_re, two_im), ("gz_0", ("gz_1", "xy_0", "xy_1")))
    correction = project_out(image_two, ritz, two_re / ritz_norm, two_im / ritz_norm)
    sensitivity = jnp.sum(correction * rho_term, axis=0) / 36.0 * mask
    deep_sens = with_halo(sensitivity, ((GZ, 0),), filter_reach)
    smooth_z = smooth_axis(deep_sens, 0, depth).reshape(depth, EY, EX)
    column = lax.axis_index(XY) % TX
    below = wide_lateral(smooth_z[:, EY - filter_reach :, :], TX)
    above = wide_lateral(smooth_z[:, :filter_reach, :], -TX)
    smooth_y = smooth_axis(jnp.concatenate([below, smooth_z, above], axis=1), 1, EY)
    left_part = jnp.where(column > 0, wide_lateral(smooth_y[:, :, EX - filter_reach :], 1), 0.0)
    right_part = jnp.where(column < TX - 1, wide_lateral(smooth_y[:, :, :filter_reach], -1), 0.0)
    smooth_x = smooth_axis(jnp.concatenate([left_part, smooth_y, right_part], axis=2), 2, EX)
    filtered = smooth_x.reshape(depth, 1, EY * EX)
    return (correction[:, :, None, :], filtered)


def solution(mesh):
    torus = Mesh(mesh.devices.reshape(4, 4, 8, 2), ("gz_0", "gz_1", "xy_0", "xy_1"))
    placed = (
        P(None, GZ, XY, None),
        P(None, GZ, XY, None),
        P(GZ, XY, None),
        P(GZ, XY, None),
        P(GZ, XY, None),
        P(),
        P(),
        P(),
        P(),
        P(),
        P(),
    )
    return jax.shard_map(
        local,
        mesh=torus,
        in_specs=placed,
        out_specs=(P(None, GZ, XY, None), P(GZ, XY, None)),
        check_vma=False,
    )
```

```python
import jax
import jax.numpy as jnp
from jax import lax
from jax.sharding import Mesh
from jax.sharding import PartitionSpec as P

TX = 4
EY = 8
EX = 16
XY = ("xy_0", "xy_1")
GZ = ("gz_0", "gz_1")


filter_reach = 5


def from_behind(x, axis, by):
    peers = lax.axis_size(axis)
    pairs = [(i, i + by) for i in range(peers) if 0 <= i + by < peers]
    return lax.ppermute(x, axis, pairs)


def with_halo(block, sides, width):
    for axis, dim in sides:
        count = lax.axis_size(axis)
        forward = [(i, i + 1) for i in range(count - 1)]
        backward = [(target, source) for source, target in forward]
        low = lax.ppermute(
            lax.slice_in_dim(block, block.shape[dim] - width, None, axis=dim), axis, forward
        )
        high = lax.ppermute(lax.slice_in_dim(block, 0, width, axis=dim), axis, backward)
        block = jnp.concatenate([low, block, high], axis=dim)
    return block


def from_everyone(x, axis):
    copies = jnp.broadcast_to(x, (lax.axis_size(axis), *x.shape))
    return lax.all_to_all(copies, axis, split_axis=0, concat_axis=0, tiled=True)


def of_everyone(x, axis):
    return from_everyone(x, axis).sum(axis=0)


def by_axis(x, axes):
    far, near = axes
    return of_everyone(x, (far, *near))


def in_one(arrays, axis):
    line, at, done = (jnp.concatenate([a.reshape(-1) for a in arrays]), 0, [])
    running = by_axis(line, axis)
    for a in arrays:
        done.append(running[at : at + a.size].reshape(a.shape))
        at += a.size
    return tuple(done)


def inner_pair(ritz, field):
    half = ritz.shape[0] // 2
    real_part = jnp.sum(ritz[:half] * field[:half] + ritz[half:] * field[half:])
    imag_part = jnp.sum(ritz[:half] * field[half:] - ritz[half:] * field[:half])
    return (real_part, imag_part)


def project_out(field, ritz, coef_re, coef_im):
    half = ritz.shape[0] // 2
    ritz_re = ritz[:half]
    ritz_im = ritz[half:]
    removed = jnp.concatenate(
        [coef_re * ritz_re - coef_im * ritz_im, coef_re * ritz_im + coef_im * ritz_re], axis=0
    )
    return field - removed


def lateral(piece, offset):
    return from_behind(piece, XY, offset)


def wide_lateral(piece, offset):
    return from_behind(piece, XY, offset)


def face_rims(field):
    blocks, depth = (field.shape[0], field.shape[1])
    grid = field.reshape(blocks, depth, EY, EX)
    z_deep = with_halo(field, ((GZ, 1),), 1)
    column = lax.axis_index(XY) % TX
    x_minus = jnp.where(column > 0, lateral(grid[:, :, :, EX - 1], 1), 0.0)
    x_plus = jnp.where(column < TX - 1, lateral(grid[:, :, :, 0], -1), 0.0)
    y_minus = lateral(grid[:, :, EY - 1, :], TX)
    y_plus = lateral(grid[:, :, 0, :], -TX)
    return (z_deep, x_minus, x_plus, y_minus, y_plus)


def flatten_cells(values):
    return values.reshape(values.shape[0], values.shape[1], EY * EX)


def assemble(field, rims):
    z_deep, x_minus, x_plus, y_minus, y_plus = rims
    blocks, depth = (field.shape[0], field.shape[1])
    grid = field.reshape(blocks, depth, EY, EX)
    x_padded = jnp.concatenate([x_minus[:, :, :, None], grid, x_plus[:, :, :, None]], axis=3)
    y_padded = jnp.concatenate([y_minus[:, :, None, :], grid, y_plus[:, :, None, :]], axis=2)
    return [
        z_deep[:, 2:],
        z_deep[:, :-2],
        flatten_cells(y_padded[:, :, 2:]),
        flatten_cells(y_padded[:, :, :-2]),
        flatten_cells(x_padded[:, :, :, 2:]),
        flatten_cells(x_padded[:, :, :, :-2]),
    ]


def matrix_apply(matrix, field):
    flat = field.reshape(field.shape[0], -1)
    return jnp.dot(
        matrix, flat, precision=lax.Precision.HIGHEST, preferred_element_type=jnp.float32
    )


def shifted_apply(field, rims, density, pml_weight, k_self, k_face, shift_re, shift_im):
    blocks = field.shape[0]
    half = blocks // 2
    self_terms = matrix_apply(k_self, field).reshape((3,) + field.shape)
    result = self_terms[0] + density * self_terms[1] + pml_weight * self_terms[2]
    neighbours = assemble(field, rims)
    for number in range(6):
        result = result + matrix_apply(k_face[number], neighbours[number]).reshape(field.shape)
    real_part = field[:half]
    imag_part = field[half:]
    result = result - jnp.concatenate(
        [shift_re * real_part - shift_im * imag_part, shift_re * imag_part + shift_im * real_part],
        axis=0,
    )
    return (result, self_terms[1])


def smooth_axis(padded, axis, length):
    result = jnp.zeros(lax.slice_in_dim(padded, 0, length, axis=axis).shape, jnp.float32)
    for offset in range(-filter_reach, filter_reach + 1):
        weight = (6.0 - abs(offset)) / 12.0
        result = result + weight * lax.slice_in_dim(
            padded, filter_reach + offset, filter_reach + offset + length, axis=axis
        )
    return result


def smooth_maps(maps, depth):
    deep = with_halo(maps, ((GZ, 1),), filter_reach)
    smooth_z = smooth_axis(deep, 1, depth).reshape(maps.shape[0], depth, EY, EX)
    column = lax.axis_index(XY) % TX
    below = wide_lateral(smooth_z[:, :, EY - filter_reach :, :], TX)
    above = wide_lateral(smooth_z[:, :, :filter_reach, :], -TX)
    smooth_y = smooth_axis(jnp.concatenate([below, smooth_z, above], axis=2), 2, EY)
    left_part = jnp.where(column > 0, wide_lateral(smooth_y[:, :, :, EX - filter_reach :], 1), 0.0)
    right_part = jnp.where(column < TX - 1, wide_lateral(smooth_y[:, :, :, :filter_reach], -1), 0.0)
    smooth_x = smooth_axis(jnp.concatenate([left_part, smooth_y, right_part], axis=3), 3, EX)
    return smooth_x.reshape(maps.shape[0], depth, EY * EX)


def local(
    residual_in,
    ritz_vector,
    density,
    pml_flags,
    design_mask,
    k_base,
    k_rho,
    k_pml,
    k_face,
    shift_re,
    shift_im,
):
    residual = residual_in[:, :, 0, :]
    ritz = ritz_vector[:, :, 0, :]
    dens = density[:, 0, :]
    pml_weight = pml_flags[:, 0, :].astype(jnp.float32)
    mask = design_mask[:, 0, :].astype(jnp.float32)
    k_self = jnp.concatenate([k_base, k_rho, k_pml], axis=0)
    blocks, depth, cells = residual.shape
    count = blocks * depth * cells * lax.axis_size(GZ) * lax.axis_size(XY)
    first_re, first_im = inner_pair(ritz, residual)
    ritz_norm, first_re, first_im = in_one(
        (jnp.sum(ritz * ritz), first_re, first_im), ("gz_0", ("gz_1", "xy_0", "xy_1"))
    )
    coef_re = first_re / ritz_norm
    coef_im = first_im / ritz_norm
    first = project_out(residual, ritz, coef_re, coef_im)
    first_rims = face_rims(first)
    image_one, unused = shifted_apply(
        first, first_rims, dens, pml_weight, k_self, k_face, shift_re, shift_im
    )
    one_re, one_im = inner_pair(ritz, image_one)
    one_re, one_im, image_sq = in_one(
        (one_re, one_im, jnp.sum(image_one * image_one)), ("gz_0", ("gz_1", "xy_0", "xy_1"))
    )
    projected = project_out(image_one, ritz, one_re / ritz_norm, one_im / ritz_norm)
    proj_sq = image_sq - (one_re * one_re + one_im * one_im) / ritz_norm
    factor = jnp.sqrt(count / proj_sq)
    second = projected * factor
    second_rims = face_rims(second)
    image_two, rho_term = shifted_apply(
        second, second_rims, dens, pml_weight, k_self, k_face, shift_re, shift_im
    )
    two_re, two_im = inner_pair(ritz, image_two)
    two_re, two_im = in_one((two_re, two_im), ("gz_0", ("gz_1", "xy_0", "xy_1")))
    half = blocks // 2
    ritz_re = ritz[:half]
    ritz_im = ritz[half:]
    rho_re = rho_term[:half]
    rho_im = rho_term[half:]
    maps = jnp.stack(
        [
            jnp.sum(image_two * rho_term, axis=0),
            jnp.sum(ritz_re * rho_re + ritz_im * rho_im, axis=0),
            jnp.sum(ritz_re * rho_im - ritz_im * rho_re, axis=0),
        ]
    ) * (mask / 36.0)
    smoothed = smooth_maps(maps, depth)
    three_re = two_re / ritz_norm
    three_im = two_im / ritz_norm
    correction = project_out(image_two, ritz, three_re, three_im)
    filtered = (smoothed[0] - three_re * smoothed[1] - three_im * smoothed[2]).reshape(depth, 1, EY * EX)
    return (correction[:, :, None, :], filtered)


def solution(mesh):
    torus = Mesh(mesh.devices.reshape(4, 4, 8, 2), ("gz_0", "gz_1", "xy_0", "xy_1"))
    placed = (
        P(None, GZ, XY, None),
        P(None, GZ, XY, None),
        P(GZ, XY, None),
        P(GZ, XY, None),
        P(GZ, XY, None),
        P(),
        P(),
        P(),
        P(),
        P(),
        P(),
    )
    return jax.shard_map(
        local,
        mesh=torus,
        in_specs=placed,
        out_specs=(P(None, GZ, XY, None), P(GZ, XY, None)),
        check_vma=False,
    )
```
